32 devices in a mesh: row: 4 (over z), col: 8 (over y, x, core).
Axes of the slice: x: 2, y: 2, z: 4, core: 2. Of those that a mesh axis runs over, the one named last changes fastest.
Arguments:
- inverse_tile: float32 [16384, 16384], P('row', 'col'), may hold values from -0.0625 to 0.0625
- factor_rows: float32 [4, 256, 16384], P(None, 'row', 'col'), may hold values from -6 to 6
- patterns: int32 [4, 128], replicated, may hold values from 0 to 1, as said below
Outputs:
- lower_columns: float32 [4, 16384, 256], P(None, ('row', 'col'))
- upper_rows: float32 [4, 256, 16384], P(None, 'col', 'row')
The draws below stay inside these ranges and needn't reach their ends.
Inputs may be any that keep to these rules, and one draw needn't show every extreme that they name: patterns[k, b] is 1 where block b of 128 ancestor rows belongs to supernode k's structure, else 0.
All inputs are finite; a program needn't handle non-finite values.
Results may differ from the reference program's by a relative error of at most 0.0001.
Values sent between devices are 32-bit elements; how exact they have to be, the bound alone decides.
No kernel may reach another device: no remote copies, remote signals or barrier semaphores. Data moves between devices by JAX's collectives and lax.ppermute only.
A program may use at most 128 MiB of HBM per device.

```python
import jax
import jax.numpy as jnp
from jax import lax

W = 256
NSUP = 4
R = 16384
NB = 128


def draw_patterns(key, part):
    scores = jax.random.randint(key, (NSUP, NB), 0, 4 * NB)
    level = jnp.arange(NB, dtype=jnp.int32)[None, :] * 3 + NB
    return (scores < level).astype(jnp.int32)


def raised(result, rng, source, target, shards_of, factor):
    def block_of(axis_at):
        return (jnp.arange(result.shape[axis_at]) // (result.shape[axis_at] // shards_of)).reshape((-1,) + (1,) * (result.ndim - 1 - axis_at))

    one_side = jax.random.permutation(rng, shards_of)[block_of(target)]
    far = (block_of(target) + shards_of // 2) % shards_of
    return jnp.where((block_of(source) == one_side) | (block_of(source) == far), factor * result, result)


def level_of(rng, dims, cuts, smallest, top_value):
    factor_of = 1.0
    for position, shards_of in cuts:
        steps = jax.random.uniform(jax.random.fold_in(jax.random.fold_in(rng, 6), position), (shards_of,), jnp.float32, smallest / len(cuts), top_value / len(cuts))
        factor_of = factor_of * jnp.repeat(jnp.exp(steps), dims[position] // shards_of).reshape((-1,) + (1,) * (len(dims) - 1 - position))
    return factor_of


def normal_values(key, shape, width, bound, shards=(), kind=jnp.bfloat16):
    result = jax.random.normal(key, shape, jnp.float32) * width
    if len(shards) > 0:
        result = level_of(key, shape, shards, -0.22, 0.18) * result
    return jnp.clip(result, min=-bound, max=bound).astype(kind)


def gaussian_with(own_key, dims, spread, limit, cuts, heavy, held_as=jnp.bfloat16):
    values = spread * jax.random.normal(own_key, dims, jnp.float32)
    if cuts:
        values = values * level_of(own_key, dims, cuts, -0.22, 0.18)
    return jnp.clip(raised(values, jax.random.fold_in(own_key, 3), *heavy), -limit, limit).astype(held_as)


def setup_inputs(seed: int = 0) -> dict:
    streams_of = jax.random.split(jax.random.key(seed), 4)
    return {
        "inverse_tile": gaussian_with(streams_of[0], (R, R), R ** -0.5, 0.0625, ((0, 4), (1, 8)), (1, 0, 8, 2.0), jnp.float32),
        "factor_rows": normal_values(streams_of[1], (NSUP, W, R), 1.0, 6.0, ((1, 4), (2, 8)), jnp.float32),
        "patterns": draw_patterns(jax.random.fold_in(streams_of[3], 71), 0),
    }


def reference(inverse_tile, factor_rows, patterns):
    keep = jnp.repeat(patterns.astype(jnp.float32), 128, axis=1)
    lower_list = []
    for number in range(NSUP):
        masked = factor_rows[number] * keep[number][None, :]
        product = lax.dot_general(inverse_tile, masked, (((1,), (1,)), ((), ())), precision=lax.Precision.HIGHEST, preferred_element_type=jnp.float32)
        lower_list.append(-(product * keep[number][:, None]))
    lower_columns = jnp.stack(lower_list)
    upper_rows = jnp.transpose(lower_columns, (0, 2, 1))
    return lower_columns, upper_rows
```

```python
import jax
import jax.numpy as jnp
from jax import lax
from jax.sharding import PartitionSpec as P


def gather_rows(block, n_row, me_row):
    h = block.shape[0]
    full = jnp.zeros((h * n_row,) + block.shape[1:], block.dtype)
    full = lax.dynamic_update_slice_in_dim(full, block, me_row * h, 0)
    for s in range(1, n_row):
        got = lax.ppermute(block, "row", [(i, (i + s) % n_row) for i in range(n_row)])
        src = (me_row - s + n_row) % n_row
        full = lax.dynamic_update_slice_in_dim(full, got, src * h, 0)
    return full


def scatter_sum_cols(part, n_col, me_col):
    n_chip = n_col // 2
    rows = part.shape[0] // n_col
    core = me_col % 2
    chip = me_col // 2
    by_dest = part.reshape(n_chip, 2, rows, part.shape[1])
    mine = lax.dynamic_index_in_dim(by_dest, core, 1, keepdims=False)
    other = lax.dynamic_index_in_dim(by_dest, 1 - core, 1, keepdims=False)
    got = lax.ppermute(other, "col", [(c, c ^ 1) for c in range(n_col)])
    chip_sum = mine + got
    total = lax.dynamic_index_in_dim(chip_sum, chip, 0, keepdims=False)
    for s in range(1, n_chip):
        dest = (chip + s) % n_chip
        piece = lax.dynamic_index_in_dim(chip_sum, dest, 0, keepdims=False)
        perm = [(c, 2 * ((c // 2 + s) % n_chip) + c % 2) for c in range(n_col)]
        total = total + lax.ppermute(piece, "col", perm)
    return total


def shards(inverse_tile, factor_rows, patterns):
    n_row = lax.axis_size("row")
    n_col = lax.axis_size("col")
    me_row = lax.axis_index("row")
    me_col = lax.axis_index("col")
    rows_here = inverse_tile.shape[0]
    cols_here = inverse_tile.shape[1]
    supernodes = factor_rows.shape[0]
    block_mask = patterns.astype(jnp.float32)
    col_blocks = cols_here // 128
    out_rows = rows_here // n_col
    out_blocks = out_rows // 128
    col_mask = jnp.repeat(
        lax.dynamic_slice_in_dim(block_mask, me_col * col_blocks, col_blocks, 1),
        128,
        axis=1,
    )
    out_mask = jnp.repeat(
        lax.dynamic_slice_in_dim(block_mask, (me_row * n_col + me_col) * out_blocks, out_blocks, 1),
        128,
        axis=1,
    )
    masked = factor_rows * col_mask[:, None, :]
    lowers = []
    uppers = []
    for number in range(supernodes):
        factor_full = gather_rows(masked[number], n_row, me_row)
        product = lax.dot_general(
            inverse_tile,
            factor_full,
            (((1,), (1,)), ((), ())),
            precision=lax.Precision.HIGHEST,
            preferred_element_type=jnp.float32,
        )
        summed = scatter_sum_cols(product, n_col, me_col)
        lower_block = -(summed * out_mask[number][:, None])
        exchanged = lax.all_to_all(lower_block[None], "col", split_axis=2, concat_axis=1, tiled=True)
        lowers.append(lower_block[None])
        uppers.append(jnp.transpose(exchanged, (0, 2, 1)))
    lower_columns = jnp.concatenate(lowers, axis=0)
    upper_rows = jnp.concatenate(uppers, axis=0)
    return (lower_columns, upper_rows)


def solution(mesh):
    in_specs = (P("row", "col"), P(None, "row", "col"), P())
    out_specs = (P(None, ("row", "col"), None), P(None, "col", "row"))
    return jax.shard_map(shards, mesh=mesh, in_specs=in_specs, out_specs=out_specs, check_vma=False)
```

```python
import jax
import jax.numpy as jnp
from jax import lax
from jax.sharding import PartitionSpec as P


def gather_rows(block, n_row, me_row):
    h = block.shape[0]
    full = jnp.zeros((h * n_row,) + block.shape[1:], block.dtype)
    full = lax.dynamic_update_slice_in_dim(full, block, me_row * h, 0)
    got_all = []
    for s in range(1, n_row):
        got = lax.ppermute(block, "row", [(i, (i + s) % n_row) for i in range(n_row)])
        src = (me_row - s + n_row) % n_row
        full = lax.dynamic_update_slice_in_dim(full, got, src * h, 0)
        got_all.append(got)
    return full, got_all


def scatter_sum_cols(part, n_col, me_col):
    n_chip = n_col // 2
    depth = part.shape[0] // n_col
    core = me_col % 2
    chip = me_col // 2
    by_dest = part.reshape(n_chip, 2, depth, part.shape[1])
    mine = lax.dynamic_index_in_dim(by_dest, core, 1, keepdims=False)
    other = lax.dynamic_index_in_dim(by_dest, 1 - core, 1, keepdims=False)
    got = lax.ppermute(other, "col", [(c, c ^ 1) for c in range(n_col)])
    chip_sum = mine + got
    total = lax.dynamic_index_in_dim(chip_sum, chip, 0, keepdims=False)
    for s in range(1, n_chip):
        dest = (chip + s) % n_chip
        piece = lax.dynamic_index_in_dim(chip_sum, dest, 0, keepdims=False)
        perm = [(c, 2 * ((c // 2 + s) % n_chip) + c % 2) for c in range(n_col)]
        total = total + lax.ppermute(piece, "col", perm)
    return total


def shards(inverse_tile, factor_rows, patterns):
    n_row = lax.axis_size("row")
    n_col = lax.axis_size("col")
    me_row = lax.axis_index("row")
    me_col = lax.axis_index("col")
    rows_here = inverse_tile.shape[0]
    cols_here = inverse_tile.shape[1]
    supernodes = factor_rows.shape[0]
    block_mask = patterns.astype(jnp.float32)
    col_blocks = cols_here // 128
    row_blocks = rows_here // 128
    col_mask = jnp.repeat(
        lax.dynamic_slice_in_dim(block_mask, me_col * col_blocks, col_blocks, 1),
        128,
        axis=1,
    )
    row_mask = jnp.repeat(
        lax.dynamic_slice_in_dim(block_mask, me_row * row_blocks, row_blocks, 1),
        128,
        axis=1,
    )
    masked = factor_rows * col_mask[:, None, :]
    lowers = []
    uppers = []
    to_send = masked[0]
    for number in range(supernodes):
        factor_full, got_all = gather_rows(to_send, n_row, me_row)
        if number + 1 < supernodes:
            to_send, _ = lax.optimization_barrier((masked[number + 1], got_all))
        product = lax.dot_general(
            factor_full,
            inverse_tile,
            (((1,), (1,)), ((), ())),
            precision=lax.Precision.HIGHEST,
            preferred_element_type=jnp.float32,
        )
        summed = scatter_sum_cols(product, n_col, me_col)
        upper_block = -(summed * row_mask[number][None, :])
        exchanged = lax.all_to_all(upper_block[None], "col", split_axis=2, concat_axis=1, tiled=True)
        uppers.append(upper_block[None])
        lowers.append(jnp.transpose(exchanged, (0, 2, 1)))
    lower_columns = jnp.concatenate(lowers, axis=0)
    upper_rows = jnp.concatenate(uppers, axis=0)
    return (lower_columns, upper_rows)


def solution(mesh):
    in_specs = (P("row", "col"), P(None, "row", "col"), P())
    out_specs = (P(None, ("row", "col"), None), P(None, "col", "row"))
    return jax.shard_map(shards, mesh=mesh, in_specs=in_specs, out_specs=out_specs, check_vma=False)
```

```python
import jax
import jax.numpy as jnp
from jax import lax
from jax.sharding import PartitionSpec as P


def gather_rows(block, n_row, me_row):
    h = block.shape[0]
    full = jnp.zeros((h * n_row,) + block.shape[1:], block.dtype)
    full = lax.dynamic_update_slice_in_dim(full, block, me_row * h, 0)
    got_all = []
    for s in range(1, n_row):
        got = lax.ppermute(block, "row", [(i, (i + s) % n_row) for i in range(n_row)])
        src = (me_row - s + n_row) % n_row
        full = lax.dynamic_update_slice_in_dim(full, got, src * h, 0)
        got_all.append(got)
    return full, got_all


def scatter_sum_cols(part, n_col, me_col):
    n_chip = n_col // 2
    depth = part.shape[0] // n_col
    core = me_col % 2
    chip = me_col // 2
    by_dest = part.reshape(n_chip, 2, depth, part.shape[1])
    mine = lax.dynamic_index_in_dim(by_dest, core, 1, keepdims=False)
    other = lax.dynamic_index_in_dim(by_dest, 1 - core, 1, keepdims=False)
    got = lax.ppermute(other, "col", [(c, c ^ 1) for c in range(n_col)])
    chip_sum = mine + got
    total = lax.dynamic_index_in_dim(chip_sum, chip, 0, keepdims=False)
    for s in range(1, n_chip):
        dest = (chip + s) % n_chip
        piece = lax.dynamic_index_in_dim(chip_sum, dest, 0, keepdims=False)
        perm = [(c, 2 * ((c // 2 + s) % n_chip) + c % 2) for c in range(n_col)]
        total = total + lax.ppermute(piece, "col", perm)
    return total


def shards(inverse_tile, factor_rows, patterns):
    n_row = lax.axis_size("row")
    n_col = lax.axis_size("col")
    me_row = lax.axis_index("row")
    me_col = lax.axis_index("col")
    rows_here = inverse_tile.shape[0]
    cols_here = inverse_tile.shape[1]
    supernodes = factor_rows.shape[0]
    block_mask = patterns.astype(jnp.float32)
    col_blocks = cols_here // 128
    row_blocks = rows_here // 128
    out_rows = rows_here // n_col
    col_mask = jnp.repeat(
        lax.dynamic_slice_in_dim(block_mask, me_col * col_blocks, col_blocks, 1),
        128,
        axis=1,
    )
    row_mask = jnp.repeat(
        lax.dynamic_slice_in_dim(block_mask, me_row * row_blocks, row_blocks, 1),
        128,
        axis=1,
    )
    masked = factor_rows * col_mask[:, None, :]
    lowers = []
    uppers = []
    to_send = masked[0]
    for number in range(supernodes):
        factor_full, got_all = gather_rows(to_send, n_row, me_row)
        if number + 1 < supernodes:
            to_send, _ = lax.optimization_barrier((masked[number + 1], got_all))
        product = lax.dot_general(
            factor_full,
            inverse_tile,
            (((1,), (1,)), ((), ())),
            precision=lax.Precision.HIGHEST,
            preferred_element_type=jnp.float32,
        )
        summed = scatter_sum_cols(product, n_col, me_col)
        upper_block = -(summed * row_mask[number][None, :])
        depth = upper_block.shape[0]
        chunks = jnp.transpose(upper_block.reshape(depth, n_col, out_rows), (1, 0, 2))
        exchanged = lax.all_to_all(chunks, "col", split_axis=0, concat_axis=0, tiled=True)
        uppers.append(upper_block[None])
        lowers.append(jnp.transpose(exchanged.reshape(n_col * depth, out_rows))[None])
    lower_columns = jnp.concatenate(lowers, axis=0)
    upper_rows = jnp.concatenate(uppers, axis=0)
    return (lower_columns, upper_rows)


def solution(mesh):
    in_specs = (P("row", "col"), P(None, "row", "col"), P())
    out_specs = (P(None, ("row", "col"), None), P(None, "col", "row"))
    return jax.shard_map(shards, mesh=mesh, in_specs=in_specs, out_specs=out_specs, check_vma=False)
```

```python
import jax
import jax.numpy as jnp
from jax import lax
from jax.sharding import PartitionSpec as P


def gather_rows(block, n_row, me_row):
    h = block.shape[0]
    full = jnp.zeros((h * n_row,) + block.shape[1:], block.dtype)
    full = lax.dynamic_update_slice_in_dim(full, block, me_row * h, 0)
    got_all = []
    for s in range(1, n_row):
        got = lax.ppermute(block, "row", [(i, (i + s) % n_row) for i in range(n_row)])
        src = (me_row - s + n_row) % n_row
        full = lax.dynamic_update_slice_in_dim(full, got, src * h, 0)
        got_all.append(got)
    return full, got_all


def sum_core_pair(part, n_col, me_col):
    n_chip = n_col // 2
    depth = part.shape[0] // n_col
    core = me_col % 2
    by_dest = part.reshape(n_chip, 2, depth, part.shape[1])
    mine = lax.dynamic_index_in_dim(by_dest, core, 1, keepdims=False)
    other = lax.dynamic_index_in_dim(by_dest, 1 - core, 1, keepdims=False)
    got = lax.ppermute(other, "col", [(c, c ^ 1) for c in range(n_col)])
    return mine + got


def sum_chips(chip_sum, n_col, me_col):
    n_chip = n_col // 2
    chip = me_col // 2
    total = lax.dynamic_index_in_dim(chip_sum, chip, 0, keepdims=False)
    for s in range(1, n_chip):
        dest = (chip + s) % n_chip
        piece = lax.dynamic_index_in_dim(chip_sum, dest, 0, keepdims=False)
        perm = [(c, 2 * ((c // 2 + s) % n_chip) + c % 2) for c in range(n_col)]
        total = total + lax.ppermute(piece, "col", perm)
    return total


def shards(inverse_tile, factor_rows, patterns):
    n_row = lax.axis_size("row")
    n_col = lax.axis_size("col")
    me_row = lax.axis_index("row")
    me_col = lax.axis_index("col")
    rows_here = inverse_tile.shape[0]
    cols_here = inverse_tile.shape[1]
    supernodes = factor_rows.shape[0]
    block_mask = patterns.astype(jnp.float32)
    col_blocks = cols_here // 128
    row_blocks = rows_here // 128
    out_rows = rows_here // n_col
    col_mask = jnp.repeat(
        lax.dynamic_slice_in_dim(block_mask, me_col * col_blocks, col_blocks, 1),
        128,
        axis=1,
    )
    row_mask = jnp.repeat(
        lax.dynamic_slice_in_dim(block_mask, me_row * row_blocks, row_blocks, 1),
        128,
        axis=1,
    )
    masked = factor_rows * col_mask[:, None, :]

    def finish(chip_sum, number):
        return -(sum_chips(chip_sum, n_col, me_col) * row_mask[number][None, :])

    def lower_of(upper_block):
        depth = upper_block.shape[0]
        chunks = jnp.transpose(upper_block.reshape(depth, n_col, out_rows), (1, 0, 2))
        exchanged = lax.all_to_all(chunks, "col", split_axis=0, concat_axis=0, tiled=True)
        return jnp.transpose(exchanged.reshape(n_col * depth, out_rows))

    last = supernodes - 1
    factor_full = gather_rows(masked[0], n_row, me_row)[0]
    pending = [masked[number] for number in range(1, supernodes)]
    products = {}
    chip_sums = {}
    uppers = {}
    lowers = {}
    for stage in range(supernodes + 2):
        state = (factor_full, pending, products, chip_sums, uppers, lowers)
        factor_full, pending, products, chip_sums, uppers, lowers = lax.optimization_barrier(state)
        products, chip_sums = dict(products), dict(chip_sums)
        uppers, lowers = dict(uppers), dict(lowers)
        ready = sorted(uppers)
        next_full = None
        if pending:
            next_full = gather_rows(pending[0], n_row, me_row)[0]
            pending = pending[1:]
        for number in sorted(chip_sums):
            uppers[number] = finish(chip_sums.pop(number), number)
        for number in sorted(products):
            chip_sums[number] = sum_core_pair(products.pop(number), n_col, me_col)
        if stage == supernodes and last in chip_sums:
            uppers[last] = finish(chip_sums.pop(last), last)
        if stage < supernodes:
            products[stage] = lax.dot_general(
                factor_full,
                inverse_tile,
                (((1,), (1,)), ((), ())),
                precision=lax.Precision.HIGHEST,
                preferred_element_type=jnp.float32,
            )
        for number in ready:
            if number not in lowers:
                lowers[number] = lower_of(uppers[number])
        factor_full = next_full if next_full is not None else jnp.zeros((), jnp.float32)
    for number in sorted(uppers):
        if number not in lowers:
            lowers[number] = lower_of(uppers[number])
    lower_columns = jnp.stack([lowers[number] for number in range(supernodes)])
    upper_rows = jnp.stack([uppers[number] for number in range(supernodes)])
    return (lower_columns, upper_rows)


def solution(mesh):
    in_specs = (P("row", "col"), P(None, "row", "col"), P())
    out_specs = (P(None, ("row", "col"), None), P(None, "col", "row"))
    return jax.shard_map(shards, mesh=mesh, in_specs=in_specs, out_specs=out_specs, check_vma=False)
```

```python
import jax
import jax.numpy as jnp
from jax import lax
from jax.sharding import PartitionSpec as P


def gather_rows(block, n_row, me_row):
    h = block.shape[0]
    full = jnp.zeros((h * n_row,) + block.shape[1:], block.dtype)
    full = lax.dynamic_update_slice_in_dim(full, block, me_row * h, 0)
    got_all = []
    for s in range(1, n_row):
        got = lax.ppermute(block, "row", [(i, (i + s) % n_row) for i in range(n_row)])
        src = (me_row - s + n_row) % n_row
        full = lax.dynamic_update_slice_in_dim(full, got, src * h, 0)
        got_all.append(got)
    return full, got_all


def sum_core_pair(part, n_col, me_col):
    n_chip = n_col // 2
    depth = part.shape[0] // n_col
    core = me_col % 2
    by_dest = part.reshape(n_chip, 2, depth, part.shape[1])
    mine = lax.dynamic_index_in_dim(by_dest, core, 1, keepdims=False)
    other = lax.dynamic_index_in_dim(by_dest, 1 - core, 1, keepdims=False)
    got = lax.ppermute(other, "col", [(c, c ^ 1) for c in range(n_col)])
    return mine + got


def sum_chips(chip_sum, n_col, me_col):
    n_chip = n_col // 2
    chip = me_col // 2
    total = lax.dynamic_index_in_dim(chip_sum, chip, 0, keepdims=False)
    for s in range(1, n_chip):
        dest = (chip + s) % n_chip
        piece = lax.dynamic_index_in_dim(chip_sum, dest, 0, keepdims=False)
        perm = [(c, 2 * ((c // 2 + s) % n_chip) + c % 2) for c in range(n_col)]
        total = total + lax.ppermute(piece, "col", perm)
    return total


def shards(inverse_tile, factor_rows, patterns):
    n_row = lax.axis_size("row")
    n_col = lax.axis_size("col")
    me_row = lax.axis_index("row")
    me_col = lax.axis_index("col")
    rows_here = inverse_tile.shape[0]
    cols_here = inverse_tile.shape[1]
    supernodes = factor_rows.shape[0]
    block_mask = patterns.astype(jnp.float32)
    col_blocks = cols_here // 128
    row_blocks = rows_here // 128
    out_rows = rows_here // n_col
    col_mask = jnp.repeat(
        lax.dynamic_slice_in_dim(block_mask, me_col * col_blocks, col_blocks, 1),
        128,
        axis=1,
    )
    row_mask = jnp.repeat(
        lax.dynamic_slice_in_dim(block_mask, me_row * row_blocks, row_blocks, 1),
        128,
        axis=1,
    )
    masked = factor_rows * col_mask[:, None, :]

    def finish(chip_sum, number):
        return -(sum_chips(chip_sum, n_col, me_col) * row_mask[number][None, :])

    def lower_of(upper_block):
        depth = upper_block.shape[0]
        chunks = jnp.transpose(upper_block.reshape(depth, n_col, out_rows), (1, 0, 2))
        exchanged = lax.all_to_all(chunks, "col", split_axis=0, concat_axis=0, tiled=True)
        return jnp.transpose(exchanged.reshape(n_col * depth, out_rows))

    last = supernodes - 1
    factor_full = gather_rows(masked[0], n_row, me_row)[0]
    pending = [masked[number] for number in range(1, supernodes)]
    products = {}
    chip_sums = {}
    uppers = {}
    lowers = {}
    for stage in range(supernodes + 2):
        if stage < supernodes:
            state = (factor_full, pending, products, chip_sums, uppers, lowers)
            factor_full, pending, products, chip_sums, uppers, lowers = lax.optimization_barrier(state)
        products, chip_sums = dict(products), dict(chip_sums)
        uppers, lowers = dict(uppers), dict(lowers)
        ready = sorted(uppers)
        next_full = None
        if pending:
            next_full = gather_rows(pending[0], n_row, me_row)[0]
            pending = pending[1:]
        for number in sorted(chip_sums):
            uppers[number] = finish(chip_sums.pop(number), number)
        for number in sorted(products):
            chip_sums[number] = sum_core_pair(products.pop(number), n_col, me_col)
        if stage == supernodes and last in chip_sums:
            uppers[last] = finish(chip_sums.pop(last), last)
        if stage < supernodes:
            products[stage] = lax.dot_general(
                factor_full,
                inverse_tile,
                (((1,), (1,)), ((), ())),
                precision=lax.Precision.HIGHEST,
                preferred_element_type=jnp.float32,
            )
        for number in ready:
            if number not in lowers:
                lowers[number] = lower_of(uppers[number])
        factor_full = next_full if next_full is not None else jnp.zeros((), jnp.float32)
    for number in sorted(uppers):
        if number not in lowers:
            lowers[number] = lower_of(uppers[number])
    lower_columns = jnp.stack([lowers[number] for number in range(supernodes)])
    upper_rows = jnp.stack([uppers[number] for number in range(supernodes)])
    return (lower_columns, upper_rows)


def solution(mesh):
    in_specs = (P("row", "col"), P(None, "row", "col"), P())
    out_specs = (P(None, ("row", "col"), None), P(None, "col", "row"))
    return jax.shard_map(shards, mesh=mesh, in_specs=in_specs, out_specs=out_specs, check_vma=False)
```

```python
import jax
import jax.numpy as jnp
from jax import lax
from jax.sharding import PartitionSpec as P


def gather_rows(block, n_row, me_row):
    h = block.shape[0]
    full = jnp.zeros((h * n_row,) + block.shape[1:], block.dtype)
    full = lax.dynamic_update_slice_in_dim(full, block, me_row * h, 0)
    got_all = []
    for s in range(1, n_row):
        got = lax.ppermute(block, "row", [(i, (i + s) % n_row) for i in range(n_row)])
        src = (me_row - s + n_row) % n_row
        full = lax.dynamic_update_slice_in_dim(full, got, src * h, 0)
        got_all.append(got)
    return full, got_all


def sum_core_pair(part, n_col, me_col):
    n_chip = n_col // 2
    depth = part.shape[0] // n_col
    core = me_col % 2
    by_dest = part.reshape(n_chip, 2, depth, part.shape[1])
    mine = lax.dynamic_index_in_dim(by_dest, core, 1, keepdims=False)
    other = lax.dynamic_index_in_dim(by_dest, 1 - core, 1, keepdims=False)
    got = lax.ppermute(other, "col", [(c, c ^ 1) for c in range(n_col)])
    return mine + got


def sum_chips(chip_sum, n_col, me_col):
    n_chip = n_col // 2
    chip = me_col // 2
    total = lax.dynamic_index_in_dim(chip_sum, chip, 0, keepdims=False)
    for s in range(1, n_chip):
        dest = (chip + s) % n_chip
        piece = lax.dynamic_index_in_dim(chip_sum, dest, 0, keepdims=False)
        perm = [(c, 2 * ((c // 2 + s) % n_chip) + c % 2) for c in range(n_col)]
        total = total + lax.ppermute(piece, "col", perm)
    return total


def shards(inverse_tile, factor_rows, patterns):
    n_row = lax.axis_size("row")
    n_col = lax.axis_size("col")
    me_row = lax.axis_index("row")
    me_col = lax.axis_index("col")
    rows_here = inverse_tile.shape[0]
    cols_here = inverse_tile.shape[1]
    supernodes = factor_rows.shape[0]
    block_mask = patterns.astype(jnp.float32)
    col_blocks = cols_here // 128
    row_blocks = rows_here // 128
    out_rows = rows_here // n_col
    col_mask = jnp.repeat(
        lax.dynamic_slice_in_dim(block_mask, me_col * col_blocks, col_blocks, 1),
        128,
        axis=1,
    )
    row_mask = jnp.repeat(
        lax.dynamic_slice_in_dim(block_mask, me_row * row_blocks, row_blocks, 1),
        128,
        axis=1,
    )
    masked = factor_rows * col_mask[:, None, :]

    def finish(chip_sum, number):
        return -(sum_chips(chip_sum, n_col, me_col) * row_mask[number][None, :])

    def lowers_of(upper_blocks):
        stacked = jnp.stack(upper_blocks)
        count, depth = stacked.shape[0], stacked.shape[1]
        chunks = jnp.transpose(stacked.reshape(count, depth, n_col, out_rows), (2, 0, 1, 3))
        exchanged = lax.all_to_all(chunks, "col", split_axis=0, concat_axis=0, tiled=True)
        return jnp.transpose(exchanged, (1, 0, 2, 3)).reshape(count, n_col * depth, out_rows).transpose(0, 2, 1)

    last = supernodes - 1
    factor_full = gather_rows(masked[0], n_row, me_row)[0]
    pending = [masked[number] for number in range(1, supernodes)]
    products = {}
    chip_sums = {}
    uppers = {}
    lowers = {}
    for stage in range(supernodes + 2):
        if stage < supernodes:
            state = (factor_full, pending, products, chip_sums, uppers, lowers)
            factor_full, pending, products, chip_sums, uppers, lowers = lax.optimization_barrier(state)
        products, chip_sums = dict(products), dict(chip_sums)
        uppers, lowers = dict(uppers), dict(lowers)
        next_full = None
        if pending:
            next_full = gather_rows(pending[0], n_row, me_row)[0]
            pending = pending[1:]
        for number in sorted(chip_sums):
            uppers[number] = finish(chip_sums.pop(number), number)
        for number in sorted(products):
            chip_sums[number] = sum_core_pair(products.pop(number), n_col, me_col)
        if stage == supernodes and last in chip_sums:
            uppers[last] = finish(chip_sums.pop(last), last)
        if stage < supernodes:
            products[stage] = lax.dot_general(
                factor_full,
                inverse_tile,
                (((1,), (1,)), ((), ())),
                precision=lax.Precision.HIGHEST,
                preferred_element_type=jnp.float32,
            )
        factor_full = next_full if next_full is not None else jnp.zeros((), jnp.float32)
    lower_columns = lowers_of([uppers[number] for number in range(supernodes)])
    upper_rows = jnp.stack([uppers[number] for number in range(supernodes)])
    return (lower_columns, upper_rows)


def solution(mesh):
    in_specs = (P("row", "col"), P(None, "row", "col"), P())
    out_specs = (P(None, ("row", "col"), None), P(None, "col", "row"))
    return jax.shard_map(shards, mesh=mesh, in_specs=in_specs, out_specs=out_specs, check_vma=False)
```

```python
import jax
import jax.numpy as jnp
from jax import lax
from jax.sharding import PartitionSpec as P


def gather_rows(block, n_row, me_row):
    h = block.shape[0]
    full = jnp.zeros((h * n_row,) + block.shape[1:], block.dtype)
    full = lax.dynamic_update_slice_in_dim(full, block, me_row * h, 0)
    got_all = []
    for s in range(1, n_row):
        got = lax.ppermute(block, "row", [(i, (i + s) % n_row) for i in range(n_row)])
        src = (me_row - s + n_row) % n_row
        full = lax.dynamic_update_slice_in_dim(full, got, src * h, 0)
        got_all.append(got)
    return full, got_all


def sum_core_pair(part, n_col, me_col):
    n_chip = n_col // 2
    depth = part.shape[0] // n_col
    core = me_col % 2
    by_dest = part.reshape(n_chip, 2, depth, part.shape[1])
    mine = lax.dynamic_index_in_dim(by_dest, core, 1, keepdims=False)
    other = lax.dynamic_index_in_dim(by_dest, 1 - core, 1, keepdims=False)
    got = lax.ppermute(other, "col", [(c, c ^ 1) for c in range(n_col)])
    return mine + got


def sum_chips(chip_sum, n_col, me_col):
    n_chip = n_col // 2
    chip = me_col // 2
    total = lax.dynamic_index_in_dim(chip_sum, chip, 0, keepdims=False)
    for s in range(1, n_chip):
        dest = (chip + s) % n_chip
        piece = lax.dynamic_index_in_dim(chip_sum, dest, 0, keepdims=False)
        perm = [(c, 2 * ((c // 2 + s) % n_chip) + c % 2) for c in range(n_col)]
        total = total + lax.ppermute(piece, "col", perm)
    return total


def shards(inverse_tile, factor_rows, patterns):
    n_row = lax.axis_size("row")
    n_col = lax.axis_size("col")
    me_row = lax.axis_index("row")
    me_col = lax.axis_index("col")
    rows_here = inverse_tile.shape[0]
    cols_here = inverse_tile.shape[1]
    supernodes = factor_rows.shape[0]
    block_mask = patterns.astype(jnp.float32)
    col_blocks = cols_here // 128
    row_blocks = rows_here // 128
    out_rows = rows_here // n_col
    col_mask = jnp.repeat(
        lax.dynamic_slice_in_dim(block_mask, me_col * col_blocks, col_blocks, 1),
        128,
        axis=1,
    )
    row_mask = jnp.repeat(
        lax.dynamic_slice_in_dim(block_mask, me_row * row_blocks, row_blocks, 1),
        128,
        axis=1,
    )
    masked = factor_rows * col_mask[:, None, :]

    def finish(chip_sum, number):
        return -(sum_chips(chip_sum, n_col, me_col) * row_mask[number][None, :])

    def lowers_of(upper_blocks):
        stacked = jnp.stack(upper_blocks)
        count, depth = stacked.shape[0], stacked.shape[1]
        chunks = jnp.transpose(stacked.reshape(count, depth, n_col, out_rows), (2, 0, 1, 3))
        exchanged = lax.all_to_all(chunks, "col", split_axis=0, concat_axis=0, tiled=True)
        return jnp.transpose(exchanged, (1, 0, 2, 3)).reshape(count, n_col * depth, out_rows).transpose(0, 2, 1)

    last = supernodes - 1
    factor_full = gather_rows(masked[0], n_row, me_row)[0]
    pending = [masked[number] for number in range(1, supernodes)]
    products = {}
    chip_sums = {}
    uppers = {}
    lowers = {}
    for stage in range(supernodes + 2):
        if stage < supernodes:
            state = (factor_full, pending, products, chip_sums, uppers, lowers)
            factor_full, pending, products, chip_sums, uppers, lowers = lax.optimization_barrier(state)
        products, chip_sums = dict(products), dict(chip_sums)
        uppers, lowers = dict(uppers), dict(lowers)
        next_full = None
        if pending:
            next_full = gather_rows(pending[0], n_row, me_row)[0]
            pending = pending[1:]
        for number in sorted(chip_sums):
            uppers[number] = finish(chip_sums.pop(number), number)
        for number in sorted(products):
            chip_sums[number] = sum_core_pair(products.pop(number), n_col, me_col)
        if stage == supernodes and last in chip_sums:
            uppers[last] = finish(chip_sums.pop(last), last)
        if stage < supernodes:
            products[stage] = lax.dot_general(
                factor_full,
                inverse_tile,
                (((1,), (1,)), ((), ())),
                precision=lax.Precision.HIGH,
                preferred_element_type=jnp.float32,
            )
        factor_full = next_full if next_full is not None else jnp.zeros((), jnp.float32)
    lower_columns = lowers_of([uppers[number] for number in range(supernodes)])
    upper_rows = jnp.stack([uppers[number] for number in range(supernodes)])
    return (lower_columns, upper_rows)


def solution(mesh):
    in_specs = (P("row", "col"), P(None, "row", "col"), P())
    out_specs = (P(None, ("row", "col"), None), P(None, "col", "row"))
    return jax.shard_map(shards, mesh=mesh, in_specs=in_specs, out_specs=out_specs, check_vma=False)
```

```python
import jax
import jax.numpy as jnp
from jax import lax
from jax.sharding import PartitionSpec as P


def gather_rows(block, n_row, me_row):
    h = block.shape[0]
    full = jnp.zeros((h * n_row,) + block.shape[1:], block.dtype)
    full = lax.dynamic_update_slice_in_dim(full, block, me_row * h, 0)
    got_all = []
    for s in range(1, n_row):
        got = lax.ppermute(block, "row", [(i, (i + s) % n_row) for i in range(n_row)])
        src = (me_row - s + n_row) % n_row
        full = lax.dynamic_update_slice_in_dim(full, got, src * h, 0)
        got_all.append(got)
    return full, got_all


def sum_core_pair(part, n_col, me_col):
    n_chip = n_col // 2
    depth = part.shape[0] // n_col
    core = me_col % 2
    by_dest = part.reshape(n_chip, 2, depth, part.shape[1])
    mine = lax.dynamic_index_in_dim(by_dest, core, 1, keepdims=False)
    other = lax.dynamic_index_in_dim(by_dest, 1 - core, 1, keepdims=False)
    got = lax.ppermute(other, "col", [(c, c ^ 1) for c in range(n_col)])
    return mine + got


def sum_chips(chip_sum, n_col, me_col):
    n_chip = n_col // 2
    chip = me_col // 2
    total = lax.dynamic_index_in_dim(chip_sum, chip, 0, keepdims=False)
    for s in range(1, n_chip):
        dest = (chip + s) % n_chip
        piece = lax.dynamic_index_in_dim(chip_sum, dest, 0, keepdims=False)
        perm = [(c, 2 * ((c // 2 + s) % n_chip) + c % 2) for c in range(n_col)]
        total = total + lax.ppermute(piece, "col", perm)
    return total


def shards(inverse_tile, factor_rows, patterns):
    n_row = lax.axis_size("row")
    n_col = lax.axis_size("col")
    me_row = lax.axis_index("row")
    me_col = lax.axis_index("col")
    rows_here = inverse_tile.shape[0]
    cols_here = inverse_tile.shape[1]
    supernodes = factor_rows.shape[0]
    block_mask = patterns.astype(jnp.float32)
    col_blocks = cols_here // 128
    row_blocks = rows_here // 128
    out_rows = rows_here // n_col
    col_mask = jnp.repeat(
        lax.dynamic_slice_in_dim(block_mask, me_col * col_blocks, col_blocks, 1),
        128,
        axis=1,
    )
    row_mask = jnp.repeat(
        lax.dynamic_slice_in_dim(block_mask, me_row * row_blocks, row_blocks, 1),
        128,
        axis=1,
    )
    masked = factor_rows * col_mask[:, None, :]

    def finish(chip_sum, number):
        return -(sum_chips(chip_sum, n_col, me_col) * row_mask[number][None, :])

    def lowers_of(upper_blocks):
        stacked = jnp.stack(upper_blocks)
        count, depth = stacked.shape[0], stacked.shape[1]
        chunks = jnp.transpose(stacked.reshape(count, depth, n_col, out_rows), (2, 0, 1, 3))
        exchanged = lax.all_to_all(chunks, "col", split_axis=0, concat_axis=0, tiled=True)
        return jnp.transpose(exchanged, (1, 0, 2, 3)).reshape(count, n_col * depth, out_rows).transpose(0, 2, 1)

    last = supernodes - 1
    factor_full = gather_rows(masked[0], n_row, me_row)[0]
    pending = [masked[number] for number in range(1, supernodes)]
    products = {}
    chip_sums = {}
    uppers = {}
    lowers = {}
    for stage in range(supernodes + 2):
        if stage < supernodes - 1:
            state = (factor_full, pending, products, chip_sums, uppers, lowers)
            factor_full, pending, products, chip_sums, uppers, lowers = lax.optimization_barrier(state)
        products, chip_sums = dict(products), dict(chip_sums)
        uppers, lowers = dict(uppers), dict(lowers)
        next_full = None
        if pending:
            next_full = gather_rows(pending[0], n_row, me_row)[0]
            pending = pending[1:]
        for number in sorted(chip_sums):
            uppers[number] = finish(chip_sums.pop(number), number)
        for number in sorted(products):
            chip_sums[number] = sum_core_pair(products.pop(number), n_col, me_col)
        if stage == supernodes and last in chip_sums:
            uppers[last] = finish(chip_sums.pop(last), last)
        if stage < supernodes:
            products[stage] = lax.dot_general(
                factor_full,
                inverse_tile,
                (((1,), (1,)), ((), ())),
                precision=lax.Precision.HIGH,
                preferred_element_type=jnp.float32,
            )
        factor_full = next_full if next_full is not None else jnp.zeros((), jnp.float32)
    early = supernodes // 2
    lower_columns = jnp.concatenate(
        [
            lowers_of([uppers[number] for number in range(early)]),
            lowers_of([uppers[number] for number in range(early, supernodes)]),
        ]
    )
    upper_rows = jnp.stack([uppers[number] for number in range(supernodes)])
    return (lower_columns, upper_rows)


def solution(mesh):
    in_specs = (P("row", "col"), P(None, "row", "col"), P())
    out_specs = (P(None, ("row", "col"), None), P(None, "col", "row"))
    return jax.shard_map(shards, mesh=mesh, in_specs=in_specs, out_specs=out_specs, check_vma=False)
```

```python
import jax
import jax.numpy as jnp
from jax import lax
from jax.sharding import PartitionSpec as P


def gather_rows(block, n_row, me_row):
    h = block.shape[0]
    full = jnp.zeros((h * n_row,) + block.shape[1:], block.dtype)
    full = lax.dynamic_update_slice_in_dim(full, block, me_row * h, 0)
    got_all = []
    for s in range(1, n_row):
        got = lax.ppermute(block, "row", [(i, (i + s) % n_row) for i in range(n_row)])
        src = (me_row - s + n_row) % n_row
        full = lax.dynamic_update_slice_in_dim(full, got, src * h, 0)
        got_all.append(got)
    return full, got_all


def sum_core_pair(part, n_col, me_col):
    n_chip = n_col // 2
    depth = part.shape[0] // n_col
    core = me_col % 2
    by_dest = part.reshape(n_chip, 2, depth, part.shape[1])
    mine = lax.dynamic_index_in_dim(by_dest, core, 1, keepdims=False)
    other = lax.dynamic_index_in_dim(by_dest, 1 - core, 1, keepdims=False)
    got = lax.ppermute(other, "col", [(c, c ^ 1) for c in range(n_col)])
    return mine + got


def sum_chips(chip_sum, n_col, me_col):
    n_chip = n_col // 2
    chip = me_col // 2
    total = lax.dynamic_index_in_dim(chip_sum, chip, 0, keepdims=False)
    for s in range(1, n_chip):
        dest = (chip + s) % n_chip
        piece = lax.dynamic_index_in_dim(chip_sum, dest, 0, keepdims=False)
        perm = [(c, 2 * ((c // 2 + s) % n_chip) + c % 2) for c in range(n_col)]
        total = total + lax.ppermute(piece, "col", perm)
    return total


def shards(inverse_tile, factor_rows, patterns):
    n_row = lax.axis_size("row")
    n_col = lax.axis_size("col")
    me_row = lax.axis_index("row")
    me_col = lax.axis_index("col")
    rows_here = inverse_tile.shape[0]
    cols_here = inverse_tile.shape[1]
    supernodes = factor_rows.shape[0]
    block_mask = patterns.astype(jnp.float32)
    col_blocks = cols_here // 128
    row_blocks = rows_here // 128
    out_rows = rows_here // n_col
    col_mask = jnp.repeat(
        lax.dynamic_slice_in_dim(block_mask, me_col * col_blocks, col_blocks, 1),
        128,
        axis=1,
    )
    row_mask = jnp.repeat(
        lax.dynamic_slice_in_dim(block_mask, me_row * row_blocks, row_blocks, 1),
        128,
        axis=1,
    )
    masked = factor_rows * col_mask[:, None, :]

    def finish(chip_sum, number):
        return -(sum_chips(chip_sum, n_col, me_col) * row_mask[number][None, :])

    def lowers_of(upper_blocks):
        stacked = jnp.stack(upper_blocks)
        count, depth = stacked.shape[0], stacked.shape[1]
        chunks = jnp.transpose(stacked.reshape(count, depth, n_col, out_rows), (2, 0, 1, 3))
        exchanged = lax.all_to_all(chunks, "col", split_axis=0, concat_axis=0, tiled=True)
        return jnp.transpose(exchanged, (1, 0, 2, 3)).reshape(count, n_col * depth, out_rows).transpose(0, 2, 1)

    last = supernodes - 1
    factor_full = gather_rows(masked[0], n_row, me_row)[0]
    pending = [masked[number] for number in range(1, supernodes)]
    chip_sums = {}
    uppers = {}
    early = None
    for stage in range(supernodes):
        state = (factor_full, pending, chip_sums, uppers)
        factor_full, pending, chip_sums, uppers = lax.optimization_barrier(state)
        chip_sums, uppers = dict(chip_sums), dict(uppers)
        next_full = None
        if pending:
            next_full = gather_rows(pending[0], n_row, me_row)[0]
            pending = pending[1:]
        for number in sorted(chip_sums):
            uppers[number] = finish(sum_core_pair(chip_sums.pop(number), n_col, me_col), number)
        product = lax.dot_general(
            factor_full,
            inverse_tile,
            (((1,), (1,)), ((), ())),
            precision=lax.Precision.HIGH,
            preferred_element_type=jnp.float32,
        )
        chip_sums[stage] = product
        if stage == last and last > 0:
            early = lowers_of([uppers[number] for number in range(last)])
        factor_full = next_full if next_full is not None else jnp.zeros((), jnp.float32)
    uppers[last] = finish(sum_core_pair(chip_sums.pop(last), n_col, me_col), last)
    tail = lowers_of([uppers[last]])
    lower_columns = tail if early is None else jnp.concatenate([early, tail])
    upper_rows = jnp.stack([uppers[number] for number in range(supernodes)])
    return (lower_columns, upper_rows)


def solution(mesh):
    in_specs = (P("row", "col"), P(None, "row", "col"), P())
    out_specs = (P(None, ("row", "col"), None), P(None, "col", "row"))
    return jax.shard_map(shards, mesh=mesh, in_specs=in_specs, out_specs=out_specs, check_vma=False)
```

```python
import jax
import jax.numpy as jnp
from jax import lax
from jax.sharding import PartitionSpec as P


def gather_rows(block, n_row, me_row):
    going_up = block
    going_down = block
    candidates = [(me_row, block)]
    for step in range(1, n_row):
        up = [(i, i + 1) for i in range(step - 1, n_row - 1)]
        down = [(i, i - 1) for i in range(1, n_row - step + 1)]
        going_up = lax.ppermute(going_up, "row", up)
        going_down = lax.ppermute(going_down, "row", down)
        candidates.append((me_row - step, going_up))
        candidates.append((me_row + step, going_down))
    pieces = []
    for source in range(n_row):
        piece = jnp.zeros_like(block)
        for at, value in candidates:
            piece = jnp.where(at == source, value, piece)
        pieces.append(piece)
    return jnp.concatenate(pieces), None


def sum_core_pair(part, n_col, me_col):
    n_chip = n_col // 2
    depth = part.shape[0] // n_col
    core = me_col % 2
    by_dest = part.reshape(n_chip, 2, depth, part.shape[1])
    mine = lax.dynamic_index_in_dim(by_dest, core, 1, keepdims=False)
    other = lax.dynamic_index_in_dim(by_dest, 1 - core, 1, keepdims=False)
    got = lax.ppermute(other, "col", [(c, c ^ 1) for c in range(n_col)])
    return mine + got


def sum_chips(chip_sum, n_col, me_col):
    n_chip = n_col // 2
    chip = me_col // 2
    total = lax.dynamic_index_in_dim(chip_sum, chip, 0, keepdims=False)
    for s in range(1, n_chip):
        dest = (chip + s) % n_chip
        piece = lax.dynamic_index_in_dim(chip_sum, dest, 0, keepdims=False)
        perm = [(c, 2 * ((c // 2 + s) % n_chip) + c % 2) for c in range(n_col)]
        total = total + lax.ppermute(piece, "col", perm)
    return total


def shards(inverse_tile, factor_rows, patterns):
    n_row = lax.axis_size("row")
    n_col = lax.axis_size("col")
    me_row = lax.axis_index("row")
    me_col = lax.axis_index("col")
    rows_here = inverse_tile.shape[0]
    cols_here = inverse_tile.shape[1]
    supernodes = factor_rows.shape[0]
    block_mask = patterns.astype(jnp.float32)
    col_blocks = cols_here // 128
    row_blocks = rows_here // 128
    out_rows = rows_here // n_col
    col_mask = jnp.repeat(
        lax.dynamic_slice_in_dim(block_mask, me_col * col_blocks, col_blocks, 1),
        128,
        axis=1,
    )
    row_mask = jnp.repeat(
        lax.dynamic_slice_in_dim(block_mask, me_row * row_blocks, row_blocks, 1),
        128,
        axis=1,
    )
    masked = factor_rows * col_mask[:, None, :]

    def finish(chip_sum, number):
        return -(sum_chips(chip_sum, n_col, me_col) * row_mask[number][None, :])

    def lowers_of(upper_blocks):
        stacked = jnp.stack(upper_blocks)
        count, depth = stacked.shape[0], stacked.shape[1]
        chunks = jnp.transpose(stacked.reshape(count, depth, n_col, out_rows), (2, 0, 1, 3))
        exchanged = lax.all_to_all(chunks, "col", split_axis=0, concat_axis=0, tiled=True)
        return jnp.transpose(exchanged, (1, 0, 2, 3)).reshape(count, n_col * depth, out_rows).transpose(0, 2, 1)

    last = supernodes - 1
    factor_full = gather_rows(masked[0], n_row, me_row)[0]
    pending = [masked[number] for number in range(1, supernodes)]
    chip_sums = {}
    uppers = {}
    early = None
    for stage in range(supernodes):
        state = (factor_full, pending, chip_sums, uppers)
        factor_full, pending, chip_sums, uppers = lax.optimization_barrier(state)
        chip_sums, uppers = dict(chip_sums), dict(uppers)
        next_full = None
        if pending:
            next_full = gather_rows(pending[0], n_row, me_row)[0]
            pending = pending[1:]
        for number in sorted(chip_sums):
            uppers[number] = finish(sum_core_pair(chip_sums.pop(number), n_col, me_col), number)
        product = lax.dot_general(
            factor_full,
            inverse_tile,
            (((1,), (1,)), ((), ())),
            precision=lax.Precision.HIGH,
            preferred_element_type=jnp.float32,
        )
        chip_sums[stage] = product
        if stage == last and last > 0:
            early = lowers_of([uppers[number] for number in range(last)])
        factor_full = next_full if next_full is not None else jnp.zeros((), jnp.float32)
    uppers[last] = finish(sum_core_pair(chip_sums.pop(last), n_col, me_col), last)
    tail = lowers_of([uppers[last]])
    lower_columns = tail if early is None else jnp.concatenate([early, tail])
    upper_rows = jnp.stack([uppers[number] for number in range(supernodes)])
    return (lower_columns, upper_rows)


def solution(mesh):
    in_specs = (P("row", "col"), P(None, "row", "col"), P())
    out_specs = (P(None, ("row", "col"), None), P(None, "col", "row"))
    return jax.shard_map(shards, mesh=mesh, in_specs=in_specs, out_specs=out_specs, check_vma=False)
```

```python
import jax
import jax.numpy as jnp
from jax import lax
from jax.sharding import PartitionSpec as P


def gather_rows(block, n_row, me_row):
    h = block.shape[0]
    full = jnp.zeros((h * n_row,) + block.shape[1:], block.dtype)
    full = lax.dynamic_update_slice_in_dim(full, block, me_row * h, 0)
    got_all = []
    for s in range(1, n_row):
        got = lax.ppermute(block, "row", [(i, (i + s) % n_row) for i in range(n_row)])
        src = (me_row - s + n_row) % n_row
        full = lax.dynamic_update_slice_in_dim(full, got, src * h, 0)
        got_all.append(got)
    return full, got_all


def sum_core_pair(part, n_col, me_col):
    n_chip = n_col // 2
    depth = part.shape[0] // n_col
    core = me_col % 2
    by_dest = part.reshape(n_chip, 2, depth, part.shape[1])
    mine = lax.dynamic_index_in_dim(by_dest, core, 1, keepdims=False)
    other = lax.dynamic_index_in_dim(by_dest, 1 - core, 1, keepdims=False)
    got = lax.ppermute(other, "col", [(c, c ^ 1) for c in range(n_col)])
    return mine + got


def sum_chips(chip_sum, n_col, me_col):
    n_chip = n_col // 2
    chip = me_col // 2
    total = lax.dynamic_index_in_dim(chip_sum, chip, 0, keepdims=False)
    for s in range(1, n_chip):
        dest = (chip + s) % n_chip
        piece = lax.dynamic_index_in_dim(chip_sum, dest, 0, keepdims=False)
        perm = [(c, 2 * ((c // 2 + s) % n_chip) + c % 2) for c in range(n_col)]
        total = total + lax.ppermute(piece, "col", perm)
    return total


def shards(inverse_tile, factor_rows, patterns):
    n_row = lax.axis_size("row")
    n_col = lax.axis_size("col")
    me_row = lax.axis_index("row")
    me_col = lax.axis_index("col")
    rows_here = inverse_tile.shape[0]
    cols_here = inverse_tile.shape[1]
    supernodes = factor_rows.shape[0]
    block_mask = patterns.astype(jnp.float32)
    col_blocks = cols_here // 128
    row_blocks = rows_here // 128
    out_rows = rows_here // n_col
    col_mask = jnp.repeat(
        lax.dynamic_slice_in_dim(block_mask, me_col * col_blocks, col_blocks, 1),
        128,
        axis=1,
    )
    row_mask = jnp.repeat(
        lax.dynamic_slice_in_dim(block_mask, me_row * row_blocks, row_blocks, 1),
        128,
        axis=1,
    )
    masked = factor_rows * col_mask[:, None, :]

    def finish(chip_sum, number):
        return -(sum_chips(chip_sum, n_col, me_col) * row_mask[number][None, :])

    def lowers_of(upper_blocks):
        stacked = jnp.stack(upper_blocks)
        count, depth = stacked.shape[0], stacked.shape[1]
        chunks = jnp.transpose(stacked.reshape(count, depth, n_col, out_rows), (2, 0, 1, 3))
        exchanged = lax.all_to_all(chunks, "col", split_axis=0, concat_axis=0, tiled=True)
        return jnp.transpose(exchanged, (1, 0, 2, 3)).reshape(count, n_col * depth, out_rows).transpose(0, 2, 1)

    last = supernodes - 1
    factor_full = gather_rows(masked[0], n_row, me_row)[0]
    pending = [masked[number] for number in range(1, supernodes)]
    chip_sums = {}
    uppers = {}
    lowers = {}
    for stage in range(supernodes):
        state = (factor_full, pending, chip_sums, uppers, lowers)
        factor_full, pending, chip_sums, uppers, lowers = lax.optimization_barrier(state)
        chip_sums, uppers, lowers = dict(chip_sums), dict(uppers), dict(lowers)
        if stage >= 2:
            lowers[stage - 2] = lowers_of([uppers[stage - 2]])
        next_full = None
        if pending:
            next_full = gather_rows(pending[0], n_row, me_row)[0]
            pending = pending[1:]
        for number in sorted(chip_sums):
            uppers[number] = finish(sum_core_pair(chip_sums.pop(number), n_col, me_col), number)
        product = lax.dot_general(
            factor_full,
            inverse_tile,
            (((1,), (1,)), ((), ())),
            precision=lax.Precision.HIGH,
            preferred_element_type=jnp.float32,
        )
        chip_sums[stage] = product
        factor_full = next_full if next_full is not None else jnp.zeros((), jnp.float32)
    uppers[last] = finish(sum_core_pair(chip_sums.pop(last), n_col, me_col), last)
    rest = [number for number in range(supernodes) if number not in lowers]
    lowers[rest[0]] = lowers_of([uppers[number] for number in rest])
    lower_columns = jnp.concatenate([lowers[number] for number in sorted(lowers)])
    upper_rows = jnp.stack([uppers[number] for number in range(supernodes)])
    return (lower_columns, upper_rows)


def solution(mesh):
    in_specs = (P("row", "col"), P(None, "row", "col"), P())
    out_specs = (P(None, ("row", "col"), None), P(None, "col", "row"))
    return jax.shard_map(shards, mesh=mesh, in_specs=in_specs, out_specs=out_specs, check_vma=False)
```

```python
import jax
import jax.numpy as jnp
from jax import lax
from jax.sharding import PartitionSpec as P


def gather_rows(block, n_row, me_row):
    h = block.shape[0]
    full = jnp.zeros((h * n_row,) + block.shape[1:], block.dtype)
    full = lax.dynamic_update_slice_in_dim(full, block, me_row * h, 0)
    got_all = []
    for s in range(1, n_row):
        got = lax.ppermute(block, "row", [(i, (i + s) % n_row) for i in range(n_row)])
        src = (me_row - s + n_row) % n_row
        full = lax.dynamic_update_slice_in_dim(full, got, src * h, 0)
        got_all.append(got)
    return full, got_all


def sum_core_pair(part, n_col, me_col):
    n_chip = n_col // 2
    depth = part.shape[0] // n_col
    core = me_col % 2
    by_dest = part.reshape(n_chip, 2, depth, part.shape[1])
    mine = lax.dynamic_index_in_dim(by_dest, core, 1, keepdims=False)
    other = lax.dynamic_index_in_dim(by_dest, 1 - core, 1, keepdims=False)
    got = lax.ppermute(other, "col", [(c, c ^ 1) for c in range(n_col)])
    return mine + got


def sum_chips(chip_sum, n_col, me_col):
    n_chip = n_col // 2
    chip = me_col // 2
    total = lax.dynamic_index_in_dim(chip_sum, chip, 0, keepdims=False)
    for s in range(1, n_chip):
        dest = (chip + s) % n_chip
        piece = lax.dynamic_index_in_dim(chip_sum, dest, 0, keepdims=False)
        perm = [(c, 2 * ((c // 2 + s) % n_chip) + c % 2) for c in range(n_col)]
        total = total + lax.ppermute(piece, "col", perm)
    return total


def shards(inverse_tile, factor_rows, patterns):
    n_row = lax.axis_size("row")
    n_col = lax.axis_size("col")
    me_row = lax.axis_index("row")
    me_col = lax.axis_index("col")
    rows_here = inverse_tile.shape[0]
    cols_here = inverse_tile.shape[1]
    supernodes = factor_rows.shape[0]
    block_mask = patterns.astype(jnp.float32)
    col_blocks = cols_here // 128
    row_blocks = rows_here // 128
    out_rows = rows_here // n_col
    col_mask = jnp.repeat(
        lax.dynamic_slice_in_dim(block_mask, me_col * col_blocks, col_blocks, 1),
        128,
        axis=1,
    )
    row_mask = jnp.repeat(
        lax.dynamic_slice_in_dim(block_mask, me_row * row_blocks, row_blocks, 1),
        128,
        axis=1,
    )
    masked = factor_rows * col_mask[:, None, :]

    def finish(chip_sum, number):
        return -(sum_chips(chip_sum, n_col, me_col) * row_mask[number][None, :])

    def lowers_of(upper_blocks):
        stacked = jnp.stack(upper_blocks)
        count, depth = stacked.shape[0], stacked.shape[1]
        chunks = jnp.transpose(stacked.reshape(count, depth, n_col, out_rows), (2, 0, 1, 3))
        exchanged = lax.all_to_all(chunks, "col", split_axis=0, concat_axis=0, tiled=True)
        return jnp.transpose(exchanged, (1, 0, 2, 3)).reshape(count, n_col * depth, out_rows).transpose(0, 2, 1)

    last = supernodes - 1
    half = masked.shape[1] // 2
    sends = [masked[0][:half], masked[0][half:]] + [masked[number] for number in range(1, supernodes)]
    owners = [0, 0] + list(range(1, supernodes))
    factor_full = gather_rows(sends[0], n_row, me_row)[0]
    pending = sends[1:]
    chip_sums = {}
    uppers = {}
    halves = {}
    for unit in range(len(sends)):
        state = (factor_full, pending, chip_sums, uppers, halves)
        factor_full, pending, chip_sums, uppers, halves = lax.optimization_barrier(state)
        chip_sums, uppers, halves = dict(chip_sums), dict(uppers), dict(halves)
        next_full = None
        if pending:
            next_full = gather_rows(pending[0], n_row, me_row)[0]
            pending = pending[1:]
        for number in sorted(chip_sums):
            uppers[number] = finish(sum_core_pair(chip_sums.pop(number), n_col, me_col), number)
        product = lax.dot_general(
            factor_full,
            inverse_tile,
            (((1,), (1,)), ((), ())),
            precision=lax.Precision.HIGH,
            preferred_element_type=jnp.float32,
        )
        if unit == 0:
            halves[0] = product
        elif unit == 1:
            first = halves.pop(0).reshape(n_row, half, product.shape[1])
            second = product.reshape(n_row, half, product.shape[1])
            chip_sums[0] = jnp.stack([first, second], axis=1).reshape(n_row * 2 * half, product.shape[1])
        else:
            chip_sums[owners[unit]] = product
        factor_full = next_full if next_full is not None else jnp.zeros((), jnp.float32)
    uppers[last] = finish(sum_core_pair(chip_sums.pop(last), n_col, me_col), last)
    early = lowers_of([uppers[number] for number in range(last)]) if last > 0 else None
    tail = lowers_of([uppers[last]])
    lower_columns = tail if early is None else jnp.concatenate([early, tail])
    upper_rows = jnp.stack([uppers[number] for number in range(supernodes)])
    return (lower_columns, upper_rows)


def solution(mesh):
    in_specs = (P("row", "col"), P(None, "row", "col"), P())
    out_specs = (P(None, ("row", "col"), None), P(None, "col", "row"))
    return jax.shard_map(shards, mesh=mesh, in_specs=in_specs, out_specs=out_specs, check_vma=False)
```

```python
import jax
import jax.numpy as jnp
from jax import lax
from jax.sharding import PartitionSpec as P


def gather_rows(block, n_row, me_row):
    h = block.shape[0]
    full = jnp.zeros((h * n_row,) + block.shape[1:], block.dtype)
    full = lax.dynamic_update_slice_in_dim(full, block, me_row * h, 0)
    got_all = []
    for s in range(1, n_row):
        got = lax.ppermute(block, "row", [(i, (i + s) % n_row) for i in range(n_row)])
        src = (me_row - s + n_row) % n_row
        full = lax.dynamic_update_slice_in_dim(full, got, src * h, 0)
        got_all.append(got)
    return full, got_all


def sum_core_pair(part, n_col, me_col):
    n_chip = n_col // 2
    depth = part.shape[0] // n_col
    core = me_col % 2
    by_dest = part.reshape(n_chip, 2, depth, part.shape[1])
    mine = lax.dynamic_index_in_dim(by_dest, core, 1, keepdims=False)
    other = lax.dynamic_index_in_dim(by_dest, 1 - core, 1, keepdims=False)
    got = lax.ppermute(other, "col", [(c, c ^ 1) for c in range(n_col)])
    return mine + got


def sum_chips(chip_sum, n_col, me_col):
    n_chip = n_col // 2
    chip = me_col // 2
    total = lax.dynamic_index_in_dim(chip_sum, chip, 0, keepdims=False)
    for s in range(1, n_chip):
        dest = (chip + s) % n_chip
        piece = lax.dynamic_index_in_dim(chip_sum, dest, 0, keepdims=False)
        perm = [(c, 2 * ((c // 2 + s) % n_chip) + c % 2) for c in range(n_col)]
        total = total + lax.ppermute(piece, "col", perm)
    return total


def shards(inverse_tile, factor_rows, patterns):
    n_row = lax.axis_size("row")
    n_col = lax.axis_size("col")
    me_row = lax.axis_index("row")
    me_col = lax.axis_index("col")
    rows_here = inverse_tile.shape[0]
    cols_here = inverse_tile.shape[1]
    supernodes = factor_rows.shape[0]
    block_mask = patterns.astype(jnp.float32)
    col_blocks = cols_here // 128
    row_blocks = rows_here // 128
    out_rows = rows_here // n_col
    col_mask = jnp.repeat(
        lax.dynamic_slice_in_dim(block_mask, me_col * col_blocks, col_blocks, 1),
        128,
        axis=1,
    )
    row_mask = jnp.repeat(
        lax.dynamic_slice_in_dim(block_mask, me_row * row_blocks, row_blocks, 1),
        128,
        axis=1,
    )
    masked = factor_rows * col_mask[:, None, :]

    def finish(chip_sum, number, mask=None):
        mask = row_mask[number] if mask is None else mask
        return -(sum_chips(chip_sum, n_col, me_col) * mask[None, :])

    def lowers_of(upper_blocks):
        stacked = jnp.stack(upper_blocks)
        count, depth = stacked.shape[0], stacked.shape[1]
        chunks = jnp.transpose(stacked.reshape(count, depth, n_col, out_rows), (2, 0, 1, 3))
        exchanged = lax.all_to_all(chunks, "col", split_axis=0, concat_axis=0, tiled=True)
        return jnp.transpose(exchanged, (1, 0, 2, 3)).reshape(count, n_col * depth, out_rows).transpose(0, 2, 1)

    split = rows_here // 2

    def multiply(factor, inverse_rows):
        return lax.dot_general(
            factor,
            inverse_rows,
            (((1,), (1,)), ((), ())),
            precision=lax.Precision.HIGH,
            preferred_element_type=jnp.float32,
        )

    last = supernodes - 1
    factor_full = gather_rows(masked[0], n_row, me_row)[0]
    pending = [masked[number] for number in range(1, supernodes)]
    chip_sums = {}
    uppers = {}
    early = None
    for stage in range(supernodes):
        state = (factor_full, pending, chip_sums, uppers)
        factor_full, pending, chip_sums, uppers = lax.optimization_barrier(state)
        chip_sums, uppers = dict(chip_sums), dict(uppers)
        next_full = None
        if pending:
            next_full = gather_rows(pending[0], n_row, me_row)[0]
            pending = pending[1:]
        for number in sorted(chip_sums):
            uppers[number] = finish(sum_core_pair(chip_sums.pop(number), n_col, me_col), number)
        if stage < last:
            chip_sums[stage] = multiply(factor_full, inverse_tile)
        else:
            first = multiply(factor_full, inverse_tile[:split])
            factor_full, first, uppers = lax.optimization_barrier((factor_full, first, uppers))
            uppers = dict(uppers)
            second = multiply(factor_full, inverse_tile[split:])
            upper_first = finish(sum_core_pair(first, n_col, me_col), last, row_mask[last][:split])
        if stage == last and last > 0:
            early = lowers_of([uppers[number] for number in range(last)])
        factor_full = next_full if next_full is not None else jnp.zeros((), jnp.float32)
    upper_second = finish(sum_core_pair(second, n_col, me_col), last, row_mask[last][split:])
    uppers[last] = jnp.concatenate([upper_first, upper_second], axis=1)
    tail = lowers_of([uppers[last]])
    lower_columns = tail if early is None else jnp.concatenate([early, tail])
    upper_rows = jnp.stack([uppers[number] for number in range(supernodes)])
    return (lower_columns, upper_rows)


def solution(mesh):
    in_specs = (P("row", "col"), P(None, "row", "col"), P())
    out_specs = (P(None, ("row", "col"), None), P(None, "col", "row"))
    return jax.shard_map(shards, mesh=mesh, in_specs=in_specs, out_specs=out_specs, check_vma=False)
```

```python
import jax
import jax.numpy as jnp
from jax import lax
from jax.sharding import PartitionSpec as P


def gather_rows(block, n_row, me_row):
    h = block.shape[0]
    full = jnp.zeros((h * n_row,) + block.shape[1:], block.dtype)
    full = lax.dynamic_update_slice_in_dim(full, block, me_row * h, 0)
    got_all = []
    for s in range(1, n_row):
        got = lax.ppermute(block, "row", [(i, (i + s) % n_row) for i in range(n_row)])
        src = (me_row - s + n_row) % n_row
        full = lax.dynamic_update_slice_in_dim(full, got, src * h, 0)
        got_all.append(got)
    return full, got_all


def sum_core_pair(part, n_col, me_col):
    n_chip = n_col // 2
    depth = part.shape[0] // n_col
    core = me_col % 2
    by_dest = part.reshape(n_chip, 2, depth, part.shape[1])
    mine = lax.dynamic_index_in_dim(by_dest, core, 1, keepdims=False)
    other = lax.dynamic_index_in_dim(by_dest, 1 - core, 1, keepdims=False)
    got = lax.ppermute(other, "col", [(c, c ^ 1) for c in range(n_col)])
    return mine + got


def sum_chips(chip_sum, n_col, me_col):
    n_chip = n_col // 2
    chip = me_col // 2
    total = lax.dynamic_index_in_dim(chip_sum, chip, 0, keepdims=False)
    for s in range(1, n_chip):
        dest = chip ^ s
        piece = lax.dynamic_index_in_dim(chip_sum, dest, 0, keepdims=False)
        perm = [(c, c ^ (2 * s)) for c in range(n_col)]
        total = total + lax.ppermute(piece, "col", perm)
    return total


def shards(inverse_tile, factor_rows, patterns):
    n_row = lax.axis_size("row")
    n_col = lax.axis_size("col")
    me_row = lax.axis_index("row")
    me_col = lax.axis_index("col")
    rows_here = inverse_tile.shape[0]
    cols_here = inverse_tile.shape[1]
    supernodes = factor_rows.shape[0]
    block_mask = patterns.astype(jnp.float32)
    col_blocks = cols_here // 128
    row_blocks = rows_here // 128
    out_rows = rows_here // n_col
    col_mask = jnp.repeat(
        lax.dynamic_slice_in_dim(block_mask, me_col * col_blocks, col_blocks, 1),
        128,
        axis=1,
    )
    row_mask = jnp.repeat(
        lax.dynamic_slice_in_dim(block_mask, me_row * row_blocks, row_blocks, 1),
        128,
        axis=1,
    )
    masked = factor_rows * col_mask[:, None, :]

    def finish(chip_sum, number):
        return -(sum_chips(chip_sum, n_col, me_col) * row_mask[number][None, :])

    def lowers_of(upper_blocks):
        stacked = jnp.stack(upper_blocks)
        count, depth = stacked.shape[0], stacked.shape[1]
        chunks = jnp.transpose(stacked.reshape(count, depth, n_col, out_rows), (2, 0, 1, 3))
        exchanged = lax.all_to_all(chunks, "col", split_axis=0, concat_axis=0, tiled=True)
        return jnp.transpose(exchanged, (1, 0, 2, 3)).reshape(count, n_col * depth, out_rows).transpose(0, 2, 1)

    last = supernodes - 1
    factor_full = gather_rows(masked[0], n_row, me_row)[0]
    pending = [masked[number] for number in range(1, supernodes)]
    chip_sums = {}
    uppers = {}
    early = None
    for stage in range(supernodes):
        state = (factor_full, pending, chip_sums, uppers)
        factor_full, pending, chip_sums, uppers = lax.optimization_barrier(state)
        chip_sums, uppers = dict(chip_sums), dict(uppers)
        next_full = None
        if pending:
            next_full = gather_rows(pending[0], n_row, me_row)[0]
            pending = pending[1:]
        for number in sorted(chip_sums):
            uppers[number] = finish(sum_core_pair(chip_sums.pop(number), n_col, me_col), number)
        product = lax.dot_general(
            factor_full,
            inverse_tile,
            (((1,), (1,)), ((), ())),
            precision=lax.Precision.HIGH,
            preferred_element_type=jnp.float32,
        )
        chip_sums[stage] = product
        if stage == last and last > 0:
            early = lowers_of([uppers[number] for number in range(last)])
        factor_full = next_full if next_full is not None else jnp.zeros((), jnp.float32)
    uppers[last] = finish(sum_core_pair(chip_sums.pop(last), n_col, me_col), last)
    tail = lowers_of([uppers[last]])
    lower_columns = tail if early is None else jnp.concatenate([early, tail])
    upper_rows = jnp.stack([uppers[number] for number in range(supernodes)])
    return (lower_columns, upper_rows)


def solution(mesh):
    in_specs = (P("row", "col"), P(None, "row", "col"), P())
    out_specs = (P(None, ("row", "col"), None), P(None, "col", "row"))
    return jax.shard_map(shards, mesh=mesh, in_specs=in_specs, out_specs=out_specs, check_vma=False)
```

```python
import jax
import jax.numpy as jnp
from jax import lax
from jax.sharding import PartitionSpec as P


def gather_rows(block, n_row, me_row):
    h = block.shape[0]
    full = jnp.zeros((h * n_row,) + block.shape[1:], block.dtype)
    full = lax.dynamic_update_slice_in_dim(full, block, me_row * h, 0)
    got_all = []
    for s in range(1, n_row):
        got = lax.ppermute(block, "row", [(i, (i + s) % n_row) for i in range(n_row)])
        src = (me_row - s + n_row) % n_row
        full = lax.dynamic_update_slice_in_dim(full, got, src * h, 0)
        got_all.append(got)
    return full, got_all


def sum_core_pair(part, n_col, me_col):
    n_chip = n_col // 2
    depth = part.shape[0] // n_col
    core = me_col % 2
    by_dest = part.reshape(n_chip, 2, depth, part.shape[1])
    mine = lax.dynamic_index_in_dim(by_dest, core, 1, keepdims=False)
    other = lax.dynamic_index_in_dim(by_dest, 1 - core, 1, keepdims=False)
    got = lax.ppermute(other, "col", [(c, c ^ 1) for c in range(n_col)])
    return mine + got


def sum_chips(chip_sum, n_col, me_col):
    n_chip = n_col // 2
    chip = me_col // 2
    total = lax.dynamic_index_in_dim(chip_sum, chip, 0, keepdims=False)
    for s in range(1, n_chip):
        dest = (chip + s) % n_chip
        piece = lax.dynamic_index_in_dim(chip_sum, dest, 0, keepdims=False)
        perm = [(c, 2 * ((c // 2 + s) % n_chip) + c % 2) for c in range(n_col)]
        total = total + lax.ppermute(piece, "col", perm)
    return total


def shards(inverse_tile, factor_rows, patterns):
    n_row = lax.axis_size("row")
    n_col = lax.axis_size("col")
    me_row = lax.axis_index("row")
    me_col = lax.axis_index("col")
    rows_here = inverse_tile.shape[0]
    cols_here = inverse_tile.shape[1]
    supernodes = factor_rows.shape[0]
    block_mask = patterns.astype(jnp.float32)
    col_blocks = cols_here // 128
    row_blocks = rows_here // 128
    out_rows = rows_here // n_col
    col_mask = jnp.repeat(
        lax.dynamic_slice_in_dim(block_mask, me_col * col_blocks, col_blocks, 1),
        128,
        axis=1,
    )
    row_mask = jnp.repeat(
        lax.dynamic_slice_in_dim(block_mask, me_row * row_blocks, row_blocks, 1),
        128,
        axis=1,
    )
    masked = factor_rows * col_mask[:, None, :]

    def finish(chip_sum, number):
        return -(sum_chips(chip_sum, n_col, me_col) * row_mask[number][None, :])

    def lowers_of(upper_blocks):
        stacked = jnp.stack(upper_blocks)
        count, depth = stacked.shape[0], stacked.shape[1]
        chunks = jnp.transpose(stacked.reshape(count, depth, n_col, out_rows), (2, 0, 1, 3))
        exchanged = lax.all_to_all(chunks, "col", split_axis=0, concat_axis=0, tiled=True)
        return jnp.transpose(exchanged, (1, 0, 2, 3)).reshape(count, n_col * depth, out_rows).transpose(0, 2, 1)

    last = supernodes - 1
    factor_full = gather_rows(masked[0], n_row, me_row)[0]
    pending = [masked[number] for number in range(1, supernodes)]
    chip_sums = {}
    uppers = {}
    for stage in range(supernodes):
        state = (factor_full, pending, chip_sums, uppers)
        factor_full, pending, chip_sums, uppers = lax.optimization_barrier(state)
        chip_sums, uppers = dict(chip_sums), dict(uppers)
        next_full = None
        if pending:
            next_full = gather_rows(pending[0], n_row, me_row)[0]
            pending = pending[1:]
        for number in sorted(chip_sums):
            uppers[number] = finish(sum_core_pair(chip_sums.pop(number), n_col, me_col), number)
        product = lax.dot_general(
            factor_full,
            inverse_tile,
            (((1,), (1,)), ((), ())),
            precision=lax.Precision.HIGH,
            preferred_element_type=jnp.float32,
        )
        chip_sums[stage] = product
        factor_full = next_full if next_full is not None else jnp.zeros((), jnp.float32)
    uppers[last] = finish(sum_core_pair(chip_sums.pop(last), n_col, me_col), last)
    lower_columns = lowers_of([uppers[number] for number in range(supernodes)])
    upper_rows = jnp.stack([uppers[number] for number in range(supernodes)])
    return (lower_columns, upper_rows)


def solution(mesh):
    in_specs = (P("row", "col"), P(None, "row", "col"), P())
    out_specs = (P(None, ("row", "col"), None), P(None, "col", "row"))
    return jax.shard_map(shards, mesh=mesh, in_specs=in_specs, out_specs=out_specs, check_vma=False)
```
